512 devices in a mesh: section: 8 (over z), ctx: 64 (over x, y, core).
Axes of the slice: x: 4, y: 8, z: 8, core: 2. Of those that a mesh axis runs over, the one named last changes fastest.
Arguments:
- earlier_span: bfloat16 [8, 8192, 4096], P('section', 'ctx'), may hold values from -6 to 6
- span_inputs: bfloat16 [8, 8192, 4096], P('section', 'ctx'), may hold values from -24 to 24
- next_inputs: bfloat16 [8192, 4096], P('ctx'), may hold values from -24 to 24
- block_list: int32 [64, 4], replicated, may hold values from -1 to 127, as said below
- q_gain: float32 [8, 4096], P('section'), may hold values from 0.5 to 8
- k_gain: float32 [8, 4096], P('section'), may hold values from -8 to 8
- out_gain: float32 [8, 4096], P('section'), may hold values from 0.5 to 2
Outputs:
- second_out: bfloat16 [8, 8192, 4096], P('section', 'ctx')
The draws below stay inside these ranges and needn't reach their ends.
Inputs may be any that keep to these rules, and one draw needn't show every extreme that they name: `block_list`: row i names key block 64 + i, then 64 + i - 1, then 1 increasing blocks r from 0 to 61, the same in every row, then the blocks 64 + r in the same order, each replaced by -1 unless it is at least 2 blocks before 64 + i. The last row has no -1.
All inputs are finite; a program needn't handle non-finite values.
Results may differ from the reference program's by a relative error of at most 0.0055.
The reference program's roundings to bfloat16 on the way count: a program that leaves them out, or rounds other values in their place, can miss the bound.
Values may be sent and summed in bfloat16 or wider, within the bound.
No kernel may reach another device: no remote copies, remote signals or barrier semaphores. Data moves between devices by JAX's collectives and lax.ppermute only.
A program may use at most 64 MiB of HBM per device.

```python
import math
import jax
import jax.numpy as jnp
from jax import lax

HEADS = 32
HD = 128
BLOCK = 128
LOCAL = 2
NR = 1
WIDTH = 4096
NQ = 64
SPAN = 8192
NSEL = 4
SECTIONS = 8


def gain_signs(key):
    flips = jax.random.randint(jax.random.fold_in(key, 11), (SECTIONS, WIDTH), 0, 2)
    return (2 * flips - 1).astype(jnp.float32)


def gain_sizes(key):
    bottom, top = (0.5, 2.0)
    return jnp.exp(jax.random.uniform(key, (SECTIONS, WIDTH), jnp.float32, math.log(bottom), math.log(top)))


def draw_q_gain(key, part):
    return gain_sizes(jax.random.fold_in(key, 21))


def draw_k_gain(key, part):
    return gain_signs(key) * gain_sizes(jax.random.fold_in(key, 22))


def draw_rows_common(key, shape):
    return jnp.clip(jax.random.normal(key, shape, jnp.float32), -6.0, 6.0)


def draw_span_inputs(key, part):
    return draw_rows_common(jax.random.fold_in(key, 31), (SECTIONS, SPAN, WIDTH)).astype(jnp.bfloat16)


def draw_next_inputs(key, part):
    return draw_rows_common(jax.random.fold_in(key, 32), (SPAN, WIDTH)).astype(jnp.bfloat16)


def draw_block_list(key, part):
    order = jax.random.permutation(jax.random.fold_in(key, 41), NQ - LOCAL)
    offsets = jnp.sort(order[:NR]).astype(jnp.int32)
    query_block = jnp.arange(NQ, dtype=jnp.int32)
    global_block = NQ + query_block
    own = global_block[:, None]
    before = (global_block - 1)[:, None]
    earlier = jnp.broadcast_to(offsets[None, :], (NQ, NR))
    later = offsets[None, :] + NQ
    later = jnp.where(later <= global_block[:, None] - LOCAL, later, -1)
    return jnp.concatenate([own, before, earlier, later], axis=1).astype(jnp.int32)


def block_levels(stream_key, shape, cuts, smallest, largest):
    loudness = 1.0
    for axis_at, shards_of in cuts:
        draws = jax.random.uniform(jax.random.fold_in(jax.random.fold_in(stream_key, 6), axis_at), (shards_of,), jnp.float32, smallest / len(cuts), largest / len(cuts))
        loudness = loudness * jnp.repeat(jnp.exp(draws), shape[axis_at] // shards_of).reshape((-1,) + (1,) * (len(shape) - 1 - axis_at))
    return loudness


def gaussian(rng, dims, spread, limit, split=(), held_as=jnp.bfloat16):
    drawn = jax.random.normal(rng, dims, jnp.float32) * spread
    if len(split) > 0:
        drawn = block_levels(rng, dims, split, -0.22, 0.18) * drawn
    return jnp.clip(drawn, min=-limit, max=limit).astype(held_as)


def setup_inputs(seed: int = 0) -> dict:
    seeds = jax.random.split(jax.random.key(seed), 8)
    earlier_span = gaussian(seeds[0], (SECTIONS, SPAN, WIDTH), 1.0, 6.0, ((0, 8), (1, 64)))
    span_inputs = draw_span_inputs(jax.random.fold_in(seeds[7], 71), 0)
    next_inputs = draw_next_inputs(jax.random.fold_in(seeds[7], 71), 0)
    block_list = draw_block_list(jax.random.fold_in(seeds[7], 71), 0)
    q_gain = draw_q_gain(jax.random.fold_in(seeds[7], 71), 0)
    k_gain = draw_k_gain(jax.random.fold_in(seeds[7], 71), 0)
    out_gain = jnp.clip(jnp.exp(math.log(2.0) - 1.3862944 * jax.random.uniform(seeds[6], (SECTIONS, WIDTH), jnp.float32) ** block_levels(seeds[6], (SECTIONS, WIDTH), ((0, 8),), -0.2, 0.2)), 0.5, 2.0)
    return dict(earlier_span=earlier_span, span_inputs=span_inputs, next_inputs=next_inputs, block_list=block_list, q_gain=q_gain, k_gain=k_gain, out_gain=out_gain)


def normalize(rows):
    widened = rows.astype(jnp.float32).reshape(rows.shape[0], HEADS, HD)
    return widened * lax.rsqrt(lax.optimization_barrier(jnp.mean(widened * widened, axis=-1, keepdims=True)) + 1e-06)

def attend_block(query_rows, key_rows, entries, global_block, gain_query, gain_key, gain_out):
    key_flat = key_rows.reshape(NSEL * BLOCK, WIDTH)
    queries = (normalize(query_rows) * gain_query.reshape(HEADS, HD) * HD ** (-0.5)).astype(jnp.bfloat16)
    keys = (normalize(key_flat) * gain_key.reshape(HEADS, HD)).astype(jnp.bfloat16)
    values = key_flat.reshape(NSEL * BLOCK, HEADS, HD)
    key_entry = jnp.repeat(entries, BLOCK)
    key_pos = jnp.arange(NSEL * BLOCK, dtype=jnp.int32) % BLOCK
    query_pos = jnp.arange(BLOCK, dtype=jnp.int32)
    allowed = (key_entry >= 0)[None, :] & ((key_entry != global_block)[None, :] | (key_pos[None, :] <= query_pos[:, None]))
    group_heads = min(HEADS, 8)
    group_count = HEADS // group_heads

    def per_group(index):
        part_query = lax.dynamic_slice_in_dim(queries, index * group_heads, group_heads, 1)
        part_keys = lax.dynamic_slice_in_dim(keys, index * group_heads, group_heads, 1)
        part_values = lax.dynamic_slice_in_dim(values, index * group_heads, group_heads, 1)
        scores = jnp.einsum('qhd,khd->hqk', part_query.astype(jnp.float32), part_keys.astype(jnp.float32))
        scores = jnp.where(allowed[None], scores, -jnp.inf)
        maxima = lax.optimization_barrier(jnp.max(scores, axis=-1, keepdims=True))
        raw = jnp.exp(scores - maxima)
        totals = lax.optimization_barrier(jnp.sum(raw, axis=-1))
        weights = raw.astype(jnp.bfloat16)
        context = jnp.einsum('hqk,khd->qhd', weights.astype(jnp.float32), part_values.astype(jnp.float32))
        return context / jnp.transpose(totals)[:, :, None]
    contexts = lax.map(per_group, jnp.arange(group_count, dtype=jnp.int32))
    contexts = jnp.transpose(contexts, (1, 0, 2, 3)).reshape(BLOCK, WIDTH)
    return (query_rows.astype(jnp.float32) + gain_out * contexts).astype(jnp.bfloat16)

def section_layer(earlier, current, block_list, gain_query, gain_key, gain_out):
    blocks_all = jnp.concatenate([earlier, current], 0).reshape(2 * NQ, BLOCK, WIDTH)
    current_blocks = current.reshape(NQ, BLOCK, WIDTH)

    def one_block(query_block):
        entries = block_list[query_block]
        picked = jnp.take(blocks_all, jnp.maximum(entries, 0).astype(jnp.int32), axis=0)
        return attend_block(current_blocks[query_block], picked, entries, NQ + query_block, gain_query, gain_key, gain_out)
    results = lax.map(one_block, jnp.arange(NQ, dtype=jnp.int32))
    return results.reshape(SPAN, WIDTH)

def reference(earlier_span, span_inputs, next_inputs, block_list, q_gain, k_gain, out_gain):
    first_out = []
    for section_id in range(SECTIONS - 1):
        first_out.append(section_layer(earlier_span[section_id], span_inputs[section_id], block_list, q_gain[section_id], k_gain[section_id], out_gain[section_id]))
    second_out = []
    for section_id in range(SECTIONS):
        incoming = next_inputs if section_id == 0 else first_out[section_id - 1]
        second_out.append(section_layer(span_inputs[section_id], incoming, block_list, q_gain[section_id], k_gain[section_id], out_gain[section_id]))
    return jnp.stack(second_out)
```

```python
import jax
import jax.numpy as jnp
from jax import lax
from jax.sharding import PartitionSpec as P

HEADS = 32
HD = 128
BLOCK = 128
LOCAL = 2
NR = 1
WIDTH = 4096
NSEL = 4


def shifted(value, axis, steps):
    count = lax.axis_size(axis)
    pairs = [(source, (source + steps) % count) for source in range(count)]
    return lax.ppermute(value, axis, pairs)


def spread(payload, axis, root):
    count = lax.axis_size(axis)
    rows = payload.shape[0]
    pieces = payload.reshape(count, rows // count, payload.shape[1])
    received = lax.all_to_all(pieces, axis, 0, 0, tiled=True)
    mine = lax.dynamic_index_in_dim(received, root, 0, keepdims=True)
    gathered = lax.all_to_all(jnp.broadcast_to(mine, pieces.shape), axis, 0, 0, tiled=True)
    return gathered.reshape(payload.shape)


def normalize(rows):
    widened = rows.astype(jnp.float32).reshape(rows.shape[0], HEADS, HD)
    return widened * lax.rsqrt(jnp.mean(widened * widened, axis=-1, keepdims=True) + 1e-06)


def attend_block(query_rows, key_rows, entries, global_block, gain_query, gain_key, gain_out):
    key_flat = key_rows.reshape(NSEL * BLOCK, WIDTH)
    queries = (normalize(query_rows) * gain_query.reshape(HEADS, HD) * HD ** (-0.5)).astype(
        jnp.bfloat16
    )
    keys = (normalize(key_flat) * gain_key.reshape(HEADS, HD)).astype(jnp.bfloat16)
    values = key_flat.reshape(NSEL * BLOCK, HEADS, HD)
    key_entry = jnp.repeat(entries, BLOCK)
    key_pos = jnp.arange(NSEL * BLOCK, dtype=jnp.int32) % BLOCK
    query_pos = jnp.arange(BLOCK, dtype=jnp.int32)
    allowed = (key_entry >= 0)[None, :] & (
        (key_entry != global_block)[None, :] | (key_pos[None, :] <= query_pos[:, None])
    )
    scores = jnp.einsum("qhd,khd->hqk", queries, keys, preferred_element_type=jnp.float32)
    scores = jnp.where(allowed[None], scores, -jnp.inf)
    maxima = jnp.max(scores, axis=-1, keepdims=True)
    raw = jnp.exp(scores - maxima)
    totals = jnp.sum(raw, axis=-1)
    weights = raw.astype(jnp.bfloat16)
    context = jnp.einsum("hqk,khd->qhd", weights, values, preferred_element_type=jnp.float32)
    contexts = (context / jnp.transpose(totals)[:, :, None]).reshape(BLOCK, WIDTH)
    return (query_rows.astype(jnp.float32) + gain_out * contexts).astype(jnp.bfloat16)


def local(earlier_span, span_inputs, next_inputs, block_list, q_gain, k_gain, out_gain):
    group_size = lax.axis_size("ctx")
    sections = lax.axis_size("section")
    position = lax.axis_index("ctx")
    section_pos = lax.axis_index("section")
    query_entries = lax.dynamic_index_in_dim(block_list, position, 0, keepdims=False)
    full_entries = block_list[group_size - 1]
    global_block = group_size + position
    gain_query = q_gain[0]
    gain_key = k_gain[0]
    gain_out = out_gain[0]
    last = position == group_size - 1

    first_earlier = earlier_span[0]
    first_current = span_inputs[0]
    root = full_entries[LOCAL] % group_size
    both = spread(jnp.concatenate([first_earlier, first_current]), "ctx", root)
    strided_earlier, strided_current = both[:BLOCK], both[BLOCK:]

    early = shifted(
        jnp.concatenate(
            [jnp.where(last, first_earlier, first_current), jnp.where(last, first_current, next_inputs)]
        ),
        "ctx",
        1,
    )
    previous_one, previous_early = early[:BLOCK], early[BLOCK:]

    key_one = jnp.stack([first_current, previous_one, strided_earlier, strided_current])
    first_result = attend_block(
        first_current, key_one, query_entries, global_block, gain_query, gain_key, gain_out
    )

    straight = [(s, s + 1) for s in range(sections - 1)]
    received = lax.ppermute(first_result, "section", straight)
    diagonal = [
        (s * group_size + i, (s + 1) * group_size + i + 1)
        for s in range(sections - 1)
        for i in range(group_size - 1)
    ]
    received_previous = lax.ppermute(first_result, ("section", "ctx"), diagonal)
    second_current = jnp.where(section_pos == 0, next_inputs, received)
    previous_two = jnp.where(
        (position == 0) | (section_pos == 0), previous_early, received_previous
    )
    later_root = full_entries[LOCAL + NR] % group_size
    strided_later = spread(second_current, "ctx", later_root)
    key_two = jnp.stack([second_current, previous_two, strided_current, strided_later])
    second_result = attend_block(
        second_current, key_two, query_entries, global_block, gain_query, gain_key, gain_out
    )
    return second_result[None]


def solution(mesh):
    in_specs = (
        P("section", "ctx", None),
        P("section", "ctx", None),
        P("ctx", None),
        P(),
        P("section", None),
        P("section", None),
        P("section", None),
    )
    out_specs = P("section", "ctx", None)
    return jax.shard_map(local, mesh=mesh, in_specs=in_specs, out_specs=out_specs, check_vma=False)
```

```python
import jax
import jax.numpy as jnp
from jax import lax
from jax.sharding import PartitionSpec as P
from jax.experimental import pallas as pl
from jax.experimental.pallas import tpu as pltpu
import functools

HEADS = 32
HD = 128
BLOCK = 128
LOCAL = 2
NR = 1
WIDTH = 4096
NSEL = 4
GROUP = 4


def shifted(value, axis, steps):
    count = lax.axis_size(axis)
    pairs = [(source, (source + steps) % count) for source in range(count)]
    return lax.ppermute(value, axis, pairs)


def spread(payload, axis, root):
    count = lax.axis_size(axis)
    rows = payload.shape[0]
    pieces = payload.reshape(count, rows // count, payload.shape[1])
    received = lax.all_to_all(pieces, axis, 0, 0, tiled=True)
    mine = lax.dynamic_index_in_dim(received, root, 0, keepdims=True)
    gathered = lax.all_to_all(jnp.broadcast_to(mine, pieces.shape), axis, 0, 0, tiled=True)
    return gathered.reshape(payload.shape)


def attend_kernel(meta_ref, q_ref, k0_ref, k1_ref, k2_ref, k3_ref, gq_ref, gk_ref, go_ref, out_ref):
    key_refs = (k0_ref, k1_ref, k2_ref, k3_ref)
    global_block = meta_ref[NSEL]
    query_pos = lax.broadcasted_iota(jnp.int32, (BLOCK, BLOCK), 0)
    key_pos = lax.broadcasted_iota(jnp.int32, (BLOCK, BLOCK), 1)
    allowed = []
    for b in range(NSEL):
        entry = meta_ref[b]
        allowed.append((entry >= 0) & ((entry != global_block) | (key_pos <= query_pos)))
    for h in range(GROUP):
        lanes = slice(h * HD, (h + 1) * HD)
        rows = q_ref[:, lanes].astype(jnp.float32)
        normed = rows * lax.rsqrt(jnp.mean(rows * rows, axis=-1, keepdims=True) + 1e-06)
        queries = (normed * gq_ref[:, lanes] * HD ** (-0.5)).astype(jnp.bfloat16)
        scores = []
        for b in range(NSEL):
            raw_keys = key_refs[b][:, lanes]
            wide = raw_keys.astype(jnp.float32)
            keys = (wide * lax.rsqrt(jnp.mean(wide * wide, axis=-1, keepdims=True) + 1e-06) * gk_ref[:, lanes]).astype(jnp.bfloat16)
            s = lax.dot_general(queries, keys, (((1,), (1,)), ((), ())), preferred_element_type=jnp.float32)
            scores.append(jnp.where(allowed[b], s, -jnp.inf))
        maxima = functools.reduce(jnp.maximum, [jnp.max(s, axis=-1, keepdims=True) for s in scores])
        raws = [jnp.exp(s - maxima) for s in scores]
        totals = functools.reduce(jnp.add, [jnp.sum(r, axis=-1, keepdims=True) for r in raws])
        context = None
        for b in range(NSEL):
            part = jnp.dot(raws[b].astype(jnp.bfloat16), key_refs[b][:, lanes], preferred_element_type=jnp.float32)
            context = part if context is None else context + part
        out_ref[:, lanes] = (rows + go_ref[:, lanes] * (context / totals)).astype(jnp.bfloat16)


def attend_pallas(query_rows, key_blocks, entries, global_block, gain_query, gain_key, gain_out):
    meta = jnp.concatenate([entries.astype(jnp.int32), jnp.reshape(global_block, (1,)).astype(jnp.int32)])
    lanes = GROUP * HD
    row_spec = pl.BlockSpec((BLOCK, lanes), lambda g, meta: (0, g))
    gain_spec = pl.BlockSpec((1, lanes), lambda g, meta: (0, g))
    grid_spec = pltpu.PrefetchScalarGridSpec(
        num_scalar_prefetch=1,
        grid=(HEADS // GROUP,),
        in_specs=[row_spec] * (1 + NSEL) + [gain_spec] * 3,
        out_specs=row_spec,
    )
    return pl.pallas_call(
        attend_kernel,
        grid_spec=grid_spec,
        out_shape=jax.ShapeDtypeStruct((BLOCK, WIDTH), jnp.bfloat16),
    )(meta, query_rows, *key_blocks, gain_query.reshape(1, WIDTH), gain_key.reshape(1, WIDTH), gain_out.reshape(1, WIDTH))


def local(earlier_span, span_inputs, next_inputs, block_list, q_gain, k_gain, out_gain):
    group_size = lax.axis_size("ctx")
    sections = lax.axis_size("section")
    position = lax.axis_index("ctx")
    section_pos = lax.axis_index("section")
    query_entries = lax.dynamic_index_in_dim(block_list, position, 0, keepdims=False)
    full_entries = block_list[group_size - 1]
    global_block = group_size + position
    gain_query = q_gain[0]
    gain_key = k_gain[0]
    gain_out = out_gain[0]
    last = position == group_size - 1

    first_earlier = earlier_span[0]
    first_current = span_inputs[0]
    root = full_entries[LOCAL] % group_size
    both = spread(jnp.concatenate([first_earlier, first_current]), "ctx", root)
    strided_earlier, strided_current = both[:BLOCK], both[BLOCK:]

    early = shifted(
        jnp.concatenate(
            [jnp.where(last, first_earlier, first_current), jnp.where(last, first_current, next_inputs)]
        ),
        "ctx",
        1,
    )
    previous_one, previous_early = early[:BLOCK], early[BLOCK:]

    key_one = (first_current, previous_one, strided_earlier, strided_current)
    first_result = attend_pallas(
        first_current, key_one, query_entries, global_block, gain_query, gain_key, gain_out
    )

    straight = [(s, s + 1) for s in range(sections - 1)]
    received = lax.ppermute(first_result, "section", straight)
    diagonal = [
        (s * group_size + i, (s + 1) * group_size + i + 1)
        for s in range(sections - 1)
        for i in range(group_size - 1)
    ]
    received_previous = lax.ppermute(first_result, ("section", "ctx"), diagonal)
    second_current = jnp.where(section_pos == 0, next_inputs, received)
    previous_two = jnp.where(
        (position == 0) | (section_pos == 0), previous_early, received_previous
    )
    later_root = full_entries[LOCAL + NR] % group_size
    strided_later = spread(second_current, "ctx", later_root)
    key_two = (second_current, previous_two, strided_current, strided_later)
    second_result = attend_pallas(
        second_current, key_two, query_entries, global_block, gain_query, gain_key, gain_out
    )
    return second_result[None]


def solution(mesh):
    in_specs = (
        P("section", "ctx", None),
        P("section", "ctx", None),
        P("ctx", None),
        P(),
        P("section", None),
        P("section", None),
        P("section", None),
    )
    out_specs = P("section", "ctx", None)
    return jax.shard_map(local, mesh=mesh, in_specs=in_specs, out_specs=out_specs, check_vma=False)
```

```python
import jax
import jax.numpy as jnp
from jax import lax
from jax.sharding import PartitionSpec as P
from jax.experimental import pallas as pl
from jax.experimental.pallas import tpu as pltpu
import functools

HEADS = 32
HD = 128
BLOCK = 128
LOCAL = 2
NR = 1
WIDTH = 4096
NSEL = 4
GROUP = 4


def shifted(value, axis, steps):
    count = lax.axis_size(axis)
    pairs = [(source, (source + steps) % count) for source in range(count)]
    return lax.ppermute(value, axis, pairs)


def scatter_piece(payload, axis, root):
    count = lax.axis_size(axis)
    rows = payload.shape[0]
    pieces = payload.reshape(count, rows // count, payload.shape[1])
    received = lax.all_to_all(pieces, axis, 0, 0, tiled=True)
    return lax.dynamic_index_in_dim(received, root, 0, keepdims=True)


def gather_pieces(piece, axis):
    count = lax.axis_size(axis)
    shape = (count,) + piece.shape[1:]
    gathered = lax.all_to_all(jnp.broadcast_to(piece, shape), axis, 0, 0, tiled=True)
    return gathered.reshape(count * piece.shape[1], piece.shape[2])


def attend_kernel(meta_ref, q_ref, k0_ref, k1_ref, k2_ref, k3_ref, gq_ref, gk_ref, go_ref, out_ref):
    key_refs = (k0_ref, k1_ref, k2_ref, k3_ref)
    global_block = meta_ref[NSEL]
    query_pos = lax.broadcasted_iota(jnp.int32, (BLOCK, BLOCK), 0)
    key_pos = lax.broadcasted_iota(jnp.int32, (BLOCK, BLOCK), 1)
    allowed = []
    for b in range(NSEL):
        entry = meta_ref[b]
        allowed.append((entry >= 0) & ((entry != global_block) | (key_pos <= query_pos)))
    for h in range(GROUP):
        lanes = slice(h * HD, (h + 1) * HD)
        rows = q_ref[:, lanes].astype(jnp.float32)
        normed = rows * lax.rsqrt(jnp.mean(rows * rows, axis=-1, keepdims=True) + 1e-06)
        queries = (normed * gq_ref[:, lanes] * HD ** (-0.5)).astype(jnp.bfloat16)
        scores = []
        for b in range(NSEL):
            raw_keys = key_refs[b][:, lanes]
            wide = raw_keys.astype(jnp.float32)
            keys = (wide * lax.rsqrt(jnp.mean(wide * wide, axis=-1, keepdims=True) + 1e-06) * gk_ref[:, lanes]).astype(jnp.bfloat16)
            s = lax.dot_general(queries, keys, (((1,), (1,)), ((), ())), preferred_element_type=jnp.float32)
            scores.append(jnp.where(allowed[b], s, -jnp.inf))
        maxima = functools.reduce(jnp.maximum, [jnp.max(s, axis=-1, keepdims=True) for s in scores])
        raws = [jnp.exp(s - maxima) for s in scores]
        totals = functools.reduce(jnp.add, [jnp.sum(r, axis=-1, keepdims=True) for r in raws])
        context = None
        for b in range(NSEL):
            part = jnp.dot(raws[b].astype(jnp.bfloat16), key_refs[b][:, lanes], preferred_element_type=jnp.float32)
            context = part if context is None else context + part
        out_ref[:, lanes] = (rows + go_ref[:, lanes] * (context / totals)).astype(jnp.bfloat16)


def attend_pallas(query_rows, key_blocks, entries, global_block, gain_query, gain_key, gain_out):
    meta = jnp.concatenate([entries.astype(jnp.int32), jnp.reshape(global_block, (1,)).astype(jnp.int32)])
    lanes = GROUP * HD

    def row_spec(block):
        return pl.BlockSpec((BLOCK, lanes), lambda g, meta: (block, g))

    gain_spec = pl.BlockSpec((1, lanes), lambda g, meta: (0, g))
    grid_spec = pltpu.PrefetchScalarGridSpec(
        num_scalar_prefetch=1,
        grid=(HEADS // GROUP,),
        in_specs=[row_spec(0)] + [row_spec(block) for _, block in key_blocks] + [gain_spec] * 3,
        out_specs=row_spec(0),
    )
    return pl.pallas_call(
        attend_kernel,
        grid_spec=grid_spec,
        out_shape=jax.ShapeDtypeStruct((BLOCK, WIDTH), jnp.bfloat16),
    )(
        meta,
        query_rows,
        *[array for array, _ in key_blocks],
        gain_query.reshape(1, WIDTH),
        gain_key.reshape(1, WIDTH),
        gain_out.reshape(1, WIDTH),
    )


def local(earlier_span, span_inputs, next_inputs, block_list, q_gain, k_gain, out_gain):
    group_size = lax.axis_size("ctx")
    sections = lax.axis_size("section")
    position = lax.axis_index("ctx")
    section_pos = lax.axis_index("section")
    query_entries = lax.dynamic_index_in_dim(block_list, position, 0, keepdims=False)
    full_entries = block_list[group_size - 1]
    global_block = group_size + position
    gain_query = q_gain[0]
    gain_key = k_gain[0]
    gain_out = out_gain[0]
    last = position == group_size - 1

    first_earlier = earlier_span[0]
    first_current = span_inputs[0]
    root = full_entries[LOCAL] % group_size
    both = gather_pieces(
        scatter_piece(jnp.concatenate([first_earlier, first_current]), "ctx", root), "ctx"
    )
    previous_one = shifted(jnp.where(last, first_earlier, first_current), "ctx", 1)
    held, both = lax.optimization_barrier((jnp.where(last, first_current, next_inputs), both))
    previous_early = shifted(held, "ctx", 1)

    key_one = ((first_current, 0), (previous_one, 0), (both, 0), (both, 1))
    first_result = attend_pallas(
        first_current, key_one, query_entries, global_block, gain_query, gain_key, gain_out
    )

    straight = [(s, s + 1) for s in range(sections - 1)]
    received = lax.ppermute(first_result, "section", straight)
    diagonal = [
        (s * group_size + i, (s + 1) * group_size + i + 1)
        for s in range(sections - 1)
        for i in range(group_size - 1)
    ]
    received_previous = lax.ppermute(first_result, ("section", "ctx"), diagonal)
    second_current = jnp.where(section_pos == 0, next_inputs, received)
    later_root = full_entries[LOCAL + NR] % group_size
    strided_later = gather_pieces(scatter_piece(second_current, "ctx", later_root), "ctx")
    previous_two = jnp.where(
        (position == 0) | (section_pos == 0), previous_early, received_previous
    )
    key_two = ((second_current, 0), (previous_two, 0), (both, 1), (strided_later, 0))
    second_result = attend_pallas(
        second_current, key_two, query_entries, global_block, gain_query, gain_key, gain_out
    )
    return second_result[None]


def solution(mesh):
    in_specs = (
        P("section", "ctx", None),
        P("section", "ctx", None),
        P("ctx", None),
        P(),
        P("section", None),
        P("section", None),
        P("section", None),
    )
    out_specs = P("section", "ctx", None)
    return jax.shard_map(local, mesh=mesh, in_specs=in_specs, out_specs=out_specs, check_vma=False)
```

```python
import jax
import jax.numpy as jnp
from jax import lax
from jax.sharding import PartitionSpec as P
from jax.experimental import pallas as pl
from jax.experimental.pallas import tpu as pltpu
import functools

HEADS = 32
HD = 128
BLOCK = 128
LOCAL = 2
NR = 1
WIDTH = 4096
NSEL = 4
GROUP = 4


def shifted(value, axis, steps):
    count = lax.axis_size(axis)
    pairs = [(source, (source + steps) % count) for source in range(count)]
    return lax.ppermute(value, axis, pairs)


def scatter_piece(payload, axis, root):
    count = lax.axis_size(axis)
    rows = payload.shape[0]
    pieces = payload.reshape(count, rows // count, payload.shape[1])
    received = lax.all_to_all(pieces, axis, 0, 0, tiled=True)
    return lax.dynamic_index_in_dim(received, root, 0, keepdims=True)


def gather_pieces(piece, axis):
    count = lax.axis_size(axis)
    shape = (count,) + piece.shape[1:]
    gathered = lax.all_to_all(jnp.broadcast_to(piece, shape), axis, 0, 0, tiled=True)
    return gathered.reshape(count * piece.shape[1], piece.shape[2])


def attend_kernel(meta_ref, q_ref, k0_ref, k1_ref, k2_ref, k3_ref, gq_ref, gk_ref, go_ref, out_ref):
    key_refs = (k0_ref, k1_ref, k2_ref, k3_ref)
    global_block = meta_ref[NSEL]
    query_pos = lax.broadcasted_iota(jnp.int32, (BLOCK, BLOCK), 0)
    key_pos = lax.broadcasted_iota(jnp.int32, (BLOCK, BLOCK), 1)
    allowed = []
    for b in range(NSEL):
        entry = meta_ref[b]
        allowed.append((entry >= 0) & ((entry != global_block) | (key_pos <= query_pos)))
    for h in range(GROUP):
        lanes = slice(h * HD, (h + 1) * HD)
        rows = q_ref[:, lanes].astype(jnp.float32)
        normed = rows * lax.rsqrt(jnp.mean(rows * rows, axis=-1, keepdims=True) + 1e-06)
        queries = (normed * gq_ref[:, lanes] * HD ** (-0.5)).astype(jnp.bfloat16)
        scores = []
        for b in range(NSEL):
            raw_keys = key_refs[b][:, lanes]
            wide = raw_keys.astype(jnp.float32)
            keys = (wide * lax.rsqrt(jnp.mean(wide * wide, axis=-1, keepdims=True) + 1e-06) * gk_ref[:, lanes]).astype(jnp.bfloat16)
            s = lax.dot_general(queries, keys, (((1,), (1,)), ((), ())), preferred_element_type=jnp.float32)
            scores.append(jnp.where(allowed[b], s, -jnp.inf))
        maxima = functools.reduce(jnp.maximum, [jnp.max(s, axis=-1, keepdims=True) for s in scores])
        raws = [jnp.exp(s - maxima) for s in scores]
        totals = functools.reduce(jnp.add, [jnp.sum(r, axis=-1, keepdims=True) for r in raws])
        context = None
        for b in range(NSEL):
            part = jnp.dot(raws[b].astype(jnp.bfloat16), key_refs[b][:, lanes], preferred_element_type=jnp.float32)
            context = part if context is None else context + part
        out_ref[:, lanes] = (rows + go_ref[:, lanes] * (context / totals)).astype(jnp.bfloat16)


def attend_pallas(query_rows, key_blocks, entries, global_block, gain_query, gain_key, gain_out):
    meta = jnp.concatenate([entries.astype(jnp.int32), jnp.reshape(global_block, (1,)).astype(jnp.int32)])
    lanes = GROUP * HD

    def row_spec(block):
        return pl.BlockSpec((BLOCK, lanes), lambda g, meta: (block, g))

    gain_spec = pl.BlockSpec((1, lanes), lambda g, meta: (0, g))
    grid_spec = pltpu.PrefetchScalarGridSpec(
        num_scalar_prefetch=1,
        grid=(HEADS // GROUP,),
        in_specs=[row_spec(0)] + [row_spec(block) for _, block in key_blocks] + [gain_spec] * 3,
        out_specs=row_spec(0),
    )
    return pl.pallas_call(
        attend_kernel,
        grid_spec=grid_spec,
        out_shape=jax.ShapeDtypeStruct((BLOCK, WIDTH), jnp.bfloat16),
    )(
        meta,
        query_rows,
        *[array for array, _ in key_blocks],
        gain_query.reshape(1, WIDTH),
        gain_key.reshape(1, WIDTH),
        gain_out.reshape(1, WIDTH),
    )


def local(earlier_span, span_inputs, next_inputs, block_list, q_gain, k_gain, out_gain):
    group_size = lax.axis_size("ctx")
    sections = lax.axis_size("section")
    position = lax.axis_index("ctx")
    section_pos = lax.axis_index("section")
    query_entries = lax.dynamic_index_in_dim(block_list, position, 0, keepdims=False)
    full_entries = block_list[group_size - 1]
    global_block = group_size + position
    gain_query = q_gain[0]
    gain_key = k_gain[0]
    gain_out = out_gain[0]
    last = position == group_size - 1

    first_earlier = earlier_span[0]
    first_current = span_inputs[0]
    root = full_entries[LOCAL] % group_size
    piece_one = scatter_piece(jnp.concatenate([first_earlier, first_current]), "ctx", root)
    previous_one = shifted(jnp.where(last, first_earlier, first_current), "ctx", 1)
    piece_one, previous_one = lax.optimization_barrier((piece_one, previous_one))
    both = gather_pieces(piece_one, "ctx")
    held, both = lax.optimization_barrier((jnp.where(last, first_current, next_inputs), both))
    previous_early = shifted(held, "ctx", 1)

    key_one = ((first_current, 0), (previous_one, 0), (both, 0), (both, 1))
    first_result = attend_pallas(
        first_current, key_one, query_entries, global_block, gain_query, gain_key, gain_out
    )

    straight = [(s, s + 1) for s in range(sections - 1)]
    received = lax.ppermute(first_result, "section", straight)
    diagonal = [
        (s * group_size + i, (s + 1) * group_size + i + 1)
        for s in range(sections - 1)
        for i in range(group_size - 1)
    ]
    received_previous = lax.ppermute(first_result, ("section", "ctx"), diagonal)
    second_current = jnp.where(section_pos == 0, next_inputs, received)
    second_current, previous_early = lax.optimization_barrier((second_current, previous_early))
    later_root = full_entries[LOCAL + NR] % group_size
    strided_later = gather_pieces(scatter_piece(second_current, "ctx", later_root), "ctx")
    previous_two = jnp.where(
        (position == 0) | (section_pos == 0), previous_early, received_previous
    )
    key_two = ((second_current, 0), (previous_two, 0), (both, 1), (strided_later, 0))
    second_result = attend_pallas(
        second_current, key_two, query_entries, global_block, gain_query, gain_key, gain_out
    )
    return second_result[None]


def solution(mesh):
    in_specs = (
        P("section", "ctx", None),
        P("section", "ctx", None),
        P("ctx", None),
        P(),
        P("section", None),
        P("section", None),
        P("section", None),
    )
    out_specs = P("section", "ctx", None)
    return jax.shard_map(local, mesh=mesh, in_specs=in_specs, out_specs=out_specs, check_vma=False)
```

```python
import jax
import jax.numpy as jnp
from jax import lax
from jax.sharding import PartitionSpec as P
from jax.experimental import pallas as pl
from jax.experimental.pallas import tpu as pltpu
import functools

HEADS = 32
HD = 128
BLOCK = 128
LOCAL = 2
NR = 1
WIDTH = 4096
NSEL = 4
GROUP = 4


def shifted(value, axis, steps):
    count = lax.axis_size(axis)
    pairs = [(source, (source + steps) % count) for source in range(count)]
    return lax.ppermute(value, axis, pairs)


def scatter_piece(payload, axis, root):
    count = lax.axis_size(axis)
    rows = payload.shape[0]
    pieces = payload.reshape(count, rows // count, payload.shape[1])
    received = lax.all_to_all(pieces, axis, 0, 0, tiled=True)
    return lax.dynamic_index_in_dim(received, root, 0, keepdims=True)


def gather_pieces(piece, axis):
    count = lax.axis_size(axis)
    shape = (count,) + piece.shape[1:]
    gathered = lax.all_to_all(jnp.broadcast_to(piece, shape), axis, 0, 0, tiled=True)
    return gathered.reshape(count * piece.shape[1], piece.shape[2])


def attend_kernel(meta_ref, q_ref, k0_ref, k1_ref, k2_ref, k3_ref, gq_ref, gk_ref, go_ref, out_ref):
    key_refs = (k0_ref, k1_ref, k2_ref, k3_ref)
    global_block = meta_ref[NSEL]
    query_pos = lax.broadcasted_iota(jnp.int32, (BLOCK, BLOCK), 0)
    key_pos = lax.broadcasted_iota(jnp.int32, (BLOCK, BLOCK), 1)
    allowed = []
    for b in range(NSEL):
        entry = meta_ref[b]
        allowed.append((entry >= 0) & ((entry != global_block) | (key_pos <= query_pos)))
    for h in range(GROUP):
        lanes = slice(h * HD, (h + 1) * HD)
        rows = q_ref[:, lanes].astype(jnp.float32)
        normed = rows * lax.rsqrt(jnp.mean(rows * rows, axis=-1, keepdims=True) + 1e-06)
        queries = (normed * gq_ref[:, lanes] * HD ** (-0.5)).astype(jnp.bfloat16)
        scores = []
        for b in range(NSEL):
            raw_keys = key_refs[b][:, lanes]
            wide = raw_keys.astype(jnp.float32)
            keys = (wide * lax.rsqrt(jnp.mean(wide * wide, axis=-1, keepdims=True) + 1e-06) * gk_ref[:, lanes]).astype(jnp.bfloat16)
            s = lax.dot_general(queries, keys, (((1,), (1,)), ((), ())), preferred_element_type=jnp.float32)
            scores.append(jnp.where(allowed[b], s, -jnp.inf))
        maxima = functools.reduce(jnp.maximum, [jnp.max(s, axis=-1, keepdims=True) for s in scores])
        raws = [jnp.exp(s - maxima) for s in scores]
        totals = functools.reduce(jnp.add, [jnp.sum(r, axis=-1, keepdims=True) for r in raws])
        context = None
        for b in range(NSEL):
            part = jnp.dot(raws[b].astype(jnp.bfloat16), key_refs[b][:, lanes], preferred_element_type=jnp.float32)
            context = part if context is None else context + part
        out_ref[:, lanes] = (rows + go_ref[:, lanes] * (context / totals)).astype(jnp.bfloat16)


def attend_pallas(query_rows, key_blocks, entries, global_block, gain_query, gain_key, gain_out):
    meta = jnp.concatenate([entries.astype(jnp.int32), jnp.reshape(global_block, (1,)).astype(jnp.int32)])
    lanes = GROUP * HD

    def row_spec(block):
        return pl.BlockSpec((BLOCK, lanes), lambda g, meta: (block, g))

    gain_spec = pl.BlockSpec((1, lanes), lambda g, meta: (0, g))
    grid_spec = pltpu.PrefetchScalarGridSpec(
        num_scalar_prefetch=1,
        grid=(HEADS // GROUP,),
        in_specs=[row_spec(0)] + [row_spec(block) for _, block in key_blocks] + [gain_spec] * 3,
        out_specs=row_spec(0),
    )
    return pl.pallas_call(
        attend_kernel,
        grid_spec=grid_spec,
        out_shape=jax.ShapeDtypeStruct((BLOCK, WIDTH), jnp.bfloat16),
    )(
        meta,
        query_rows,
        *[array for array, _ in key_blocks],
        gain_query.reshape(1, WIDTH),
        gain_key.reshape(1, WIDTH),
        gain_out.reshape(1, WIDTH),
    )


def local(earlier_span, span_inputs, next_inputs, block_list, q_gain, k_gain, out_gain):
    group_size = lax.axis_size("ctx")
    sections = lax.axis_size("section")
    position = lax.axis_index("ctx")
    section_pos = lax.axis_index("section")
    query_entries = lax.dynamic_index_in_dim(block_list, position, 0, keepdims=False)
    full_entries = block_list[group_size - 1]
    global_block = group_size + position
    gain_query = q_gain[0]
    gain_key = k_gain[0]
    gain_out = out_gain[0]
    last = position == group_size - 1

    first_earlier = earlier_span[0]
    first_current = span_inputs[0]
    root = full_entries[LOCAL] % group_size
    piece_one = scatter_piece(jnp.concatenate([first_earlier, first_current]), "ctx", root)
    previous_one = shifted(jnp.where(last, first_earlier, first_current), "ctx", 1)
    piece_one, previous_one = lax.optimization_barrier((piece_one, previous_one))
    both = gather_pieces(piece_one, "ctx")
    held, both = lax.optimization_barrier((jnp.where(last, first_current, next_inputs), both))
    previous_early = shifted(held, "ctx", 1)

    key_one = ((first_current, 0), (previous_one, 0), (both, 0), (both, 1))
    first_result = attend_pallas(
        first_current, key_one, query_entries, global_block, gain_query, gain_key, gain_out
    )

    later_root = full_entries[LOCAL + NR] % group_size
    source = jnp.where(section_pos == sections - 1, next_inputs, first_result)
    source, previous_early = lax.optimization_barrier((source, previous_early))
    piece = shifted(scatter_piece(source, "ctx", later_root), "section", 1)
    outgoing, piece = lax.optimization_barrier((first_result, piece))
    straight = [(s, s + 1) for s in range(sections - 1)]
    received = lax.ppermute(outgoing, "section", straight)
    diagonal = [
        (s * group_size + i, (s + 1) * group_size + i + 1)
        for s in range(sections - 1)
        for i in range(group_size - 1)
    ]
    received_previous = lax.ppermute(outgoing, ("section", "ctx"), diagonal)
    strided_later = gather_pieces(piece, "ctx")
    second_current = jnp.where(section_pos == 0, next_inputs, received)
    previous_two = jnp.where(
        (position == 0) | (section_pos == 0), previous_early, received_previous
    )
    key_two = ((second_current, 0), (previous_two, 0), (both, 1), (strided_later, 0))
    second_result = attend_pallas(
        second_current, key_two, query_entries, global_block, gain_query, gain_key, gain_out
    )
    return second_result[None]


def solution(mesh):
    in_specs = (
        P("section", "ctx", None),
        P("section", "ctx", None),
        P("ctx", None),
        P(),
        P("section", None),
        P("section", None),
        P("section", None),
    )
    out_specs = P("section", "ctx", None)
    return jax.shard_map(local, mesh=mesh, in_specs=in_specs, out_specs=out_specs, check_vma=False)
```

```python
import jax
import jax.numpy as jnp
from jax import lax
from jax.sharding import PartitionSpec as P
from jax.experimental import pallas as pl
from jax.experimental.pallas import tpu as pltpu
import functools

HEADS = 32
HD = 128
BLOCK = 128
LOCAL = 2
NR = 1
WIDTH = 4096
NSEL = 4
GROUP = 8


def shifted(value, axis, steps):
    count = lax.axis_size(axis)
    pairs = [(source, (source + steps) % count) for source in range(count)]
    return lax.ppermute(value, axis, pairs)


def scatter_piece(payload, axis, root):
    count = lax.axis_size(axis)
    rows = payload.shape[0]
    pieces = payload.reshape(count, rows // count, payload.shape[1])
    received = lax.all_to_all(pieces, axis, 0, 0, tiled=True)
    return lax.dynamic_index_in_dim(received, root, 0, keepdims=True)


def gather_pieces(piece, axis):
    count = lax.axis_size(axis)
    shape = (count,) + piece.shape[1:]
    gathered = lax.all_to_all(jnp.broadcast_to(piece, shape), axis, 0, 0, tiled=True)
    return gathered.reshape(count * piece.shape[1], piece.shape[2])


def attend_kernel(meta_ref, q_ref, k0_ref, k1_ref, k2_ref, k3_ref, gq_ref, gk_ref, go_ref, out_ref):
    key_refs = (k0_ref, k1_ref, k2_ref, k3_ref)
    global_block = meta_ref[NSEL]
    query_pos = lax.broadcasted_iota(jnp.int32, (BLOCK, BLOCK), 0)
    key_pos = lax.broadcasted_iota(jnp.int32, (BLOCK, BLOCK), 1)
    allowed = []
    for b in range(NSEL):
        entry = meta_ref[b]
        allowed.append((entry >= 0) & ((entry != global_block) | (key_pos <= query_pos)))
    for h in range(GROUP):
        lanes = slice(h * HD, (h + 1) * HD)
        rows = q_ref[:, lanes].astype(jnp.float32)
        normed = rows * lax.rsqrt(jnp.mean(rows * rows, axis=-1, keepdims=True) + 1e-06)
        queries = (normed * gq_ref[:, lanes] * HD ** (-0.5)).astype(jnp.bfloat16)
        scores = []
        for b in range(NSEL):
            raw_keys = key_refs[b][:, lanes]
            wide = raw_keys.astype(jnp.float32)
            keys = (wide * lax.rsqrt(jnp.mean(wide * wide, axis=-1, keepdims=True) + 1e-06) * gk_ref[:, lanes]).astype(jnp.bfloat16)
            s = lax.dot_general(queries, keys, (((1,), (1,)), ((), ())), preferred_element_type=jnp.float32)
            scores.append(jnp.where(allowed[b], s, -jnp.inf))
        maxima = functools.reduce(jnp.maximum, [jnp.max(s, axis=-1, keepdims=True) for s in scores])
        raws = [jnp.exp(s - maxima) for s in scores]
        totals = functools.reduce(jnp.add, [jnp.sum(r, axis=-1, keepdims=True) for r in raws])
        context = None
        for b in range(NSEL):
            part = jnp.dot(raws[b].astype(jnp.bfloat16), key_refs[b][:, lanes], preferred_element_type=jnp.float32)
            context = part if context is None else context + part
        out_ref[:, lanes] = (rows + go_ref[:, lanes] * (context / totals)).astype(jnp.bfloat16)


def attend_pallas(query_rows, key_blocks, entries, global_block, gain_query, gain_key, gain_out):
    meta = jnp.concatenate([entries.astype(jnp.int32), jnp.reshape(global_block, (1,)).astype(jnp.int32)])
    lanes = GROUP * HD

    def row_spec(block):
        return pl.BlockSpec((BLOCK, lanes), lambda g, meta: (block, g))

    gain_spec = pl.BlockSpec((1, lanes), lambda g, meta: (0, g))
    grid_spec = pltpu.PrefetchScalarGridSpec(
        num_scalar_prefetch=1,
        grid=(HEADS // GROUP,),
        in_specs=[row_spec(0)] + [row_spec(block) for _, block in key_blocks] + [gain_spec] * 3,
        out_specs=row_spec(0),
    )
    return pl.pallas_call(
        attend_kernel,
        grid_spec=grid_spec,
        out_shape=jax.ShapeDtypeStruct((BLOCK, WIDTH), jnp.bfloat16),
    )(
        meta,
        query_rows,
        *[array for array, _ in key_blocks],
        gain_query.reshape(1, WIDTH),
        gain_key.reshape(1, WIDTH),
        gain_out.reshape(1, WIDTH),
    )


def local(earlier_span, span_inputs, next_inputs, block_list, q_gain, k_gain, out_gain):
    group_size = lax.axis_size("ctx")
    sections = lax.axis_size("section")
    position = lax.axis_index("ctx")
    section_pos = lax.axis_index("section")
    query_entries = lax.dynamic_index_in_dim(block_list, position, 0, keepdims=False)
    full_entries = block_list[group_size - 1]
    global_block = group_size + position
    gain_query = q_gain[0]
    gain_key = k_gain[0]
    gain_out = out_gain[0]
    last = position == group_size - 1

    first_earlier = earlier_span[0]
    first_current = span_inputs[0]
    root = full_entries[LOCAL] % group_size
    piece_one = scatter_piece(jnp.concatenate([first_earlier, first_current]), "ctx", root)
    behind = jnp.where(last, first_earlier, first_current)
    front = shifted(behind[: BLOCK // 2], "ctx", 1)
    piece_one, front = lax.optimization_barrier((piece_one, front))
    back = shifted(behind[BLOCK // 2 :], "ctx", 1)
    both = gather_pieces(piece_one, "ctx")
    both, back = lax.optimization_barrier((both, back))
    previous_one = jnp.concatenate([front, back])
    held, both = lax.optimization_barrier((jnp.where(last, first_current, next_inputs), both))
    previous_early = shifted(held, "ctx", 1)

    key_one = ((first_current, 0), (previous_one, 0), (both, 0), (both, 1))
    first_result = attend_pallas(
        first_current, key_one, query_entries, global_block, gain_query, gain_key, gain_out
    )

    later_root = full_entries[LOCAL + NR] % group_size
    source = jnp.where(section_pos == sections - 1, next_inputs, first_result)
    source, previous_early = lax.optimization_barrier((source, previous_early))
    piece = shifted(scatter_piece(source, "ctx", later_root), "section", 1)
    outgoing, piece = lax.optimization_barrier((first_result, piece))
    straight = [(s, s + 1) for s in range(sections - 1)]
    received = lax.ppermute(outgoing, "section", straight)
    diagonal = [
        (s * group_size + i, (s + 1) * group_size + i + 1)
        for s in range(sections - 1)
        for i in range(group_size - 1)
    ]
    received_previous = lax.ppermute(outgoing, ("section", "ctx"), diagonal)
    strided_later = gather_pieces(piece, "ctx")
    second_current = jnp.where(section_pos == 0, next_inputs, received)
    previous_two = jnp.where(
        (position == 0) | (section_pos == 0), previous_early, received_previous
    )
    key_two = ((second_current, 0), (previous_two, 0), (both, 1), (strided_later, 0))
    second_result = attend_pallas(
        second_current, key_two, query_entries, global_block, gain_query, gain_key, gain_out
    )
    return second_result[None]


def solution(mesh):
    in_specs = (
        P("section", "ctx", None),
        P("section", "ctx", None),
        P("ctx", None),
        P(),
        P("section", None),
        P("section", None),
        P("section", None),
    )
    out_specs = P("section", "ctx", None)
    return jax.shard_map(local, mesh=mesh, in_specs=in_specs, out_specs=out_specs, check_vma=False)
```

```python
import jax
import jax.numpy as jnp
from jax import lax
from jax.sharding import PartitionSpec as P
from jax.experimental import pallas as pl
from jax.experimental.pallas import tpu as pltpu
import functools

HEADS = 32
HD = 128
BLOCK = 128
LOCAL = 2
NR = 1
WIDTH = 4096
NSEL = 4
GROUP = 8


def shifted(value, axis, steps):
    count = lax.axis_size(axis)
    pairs = [(source, (source + steps) % count) for source in range(count)]
    return lax.ppermute(value, axis, pairs)


def scatter_piece(payload, axis, root):
    count = lax.axis_size(axis)
    rows = payload.shape[0]
    pieces = payload.reshape(count, rows // count, payload.shape[1])
    received = lax.all_to_all(pieces, axis, 0, 0, tiled=True)
    return lax.dynamic_index_in_dim(received, root, 0, keepdims=True)


def gather_pieces(piece, axis):
    count = lax.axis_size(axis)
    shape = (count,) + piece.shape[1:]
    gathered = lax.all_to_all(jnp.broadcast_to(piece, shape), axis, 0, 0, tiled=True)
    return gathered.reshape(count * piece.shape[1], piece.shape[2])


def attend_kernel(meta_ref, q_ref, k0_ref, k1a_ref, k1b_ref, k2_ref, k3_ref, gq_ref, gk_ref, go_ref, out_ref):
    key_refs = (k0_ref, (k1a_ref, k1b_ref), k2_ref, k3_ref)

    def key_rows(b, lanes):
        ref = key_refs[b]
        if isinstance(ref, tuple):
            return jnp.concatenate([part[:, lanes] for part in ref], axis=0)
        return ref[:, lanes]

    global_block = meta_ref[NSEL]
    query_pos = lax.broadcasted_iota(jnp.int32, (BLOCK, BLOCK), 0)
    key_pos = lax.broadcasted_iota(jnp.int32, (BLOCK, BLOCK), 1)
    allowed = []
    for b in range(NSEL):
        entry = meta_ref[b]
        allowed.append((entry >= 0) & ((entry != global_block) | (key_pos <= query_pos)))
    for h in range(GROUP):
        lanes = slice(h * HD, (h + 1) * HD)
        rows = q_ref[:, lanes].astype(jnp.float32)
        normed = rows * lax.rsqrt(jnp.mean(rows * rows, axis=-1, keepdims=True) + 1e-06)
        queries = (normed * gq_ref[:, lanes] * HD ** (-0.5)).astype(jnp.bfloat16)
        scores = []
        values = [key_rows(b, lanes) for b in range(NSEL)]
        for b in range(NSEL):
            raw_keys = values[b]
            wide = raw_keys.astype(jnp.float32)
            keys = (wide * lax.rsqrt(jnp.mean(wide * wide, axis=-1, keepdims=True) + 1e-06) * gk_ref[:, lanes]).astype(jnp.bfloat16)
            s = lax.dot_general(queries, keys, (((1,), (1,)), ((), ())), preferred_element_type=jnp.float32)
            scores.append(jnp.where(allowed[b], s, -jnp.inf))
        maxima = functools.reduce(jnp.maximum, [jnp.max(s, axis=-1, keepdims=True) for s in scores])
        raws = [jnp.exp(s - maxima) for s in scores]
        totals = functools.reduce(jnp.add, [jnp.sum(r, axis=-1, keepdims=True) for r in raws])
        context = None
        for b in range(NSEL):
            part = jnp.dot(raws[b].astype(jnp.bfloat16), values[b], preferred_element_type=jnp.float32)
            context = part if context is None else context + part
        out_ref[:, lanes] = (rows + go_ref[:, lanes] * (context / totals)).astype(jnp.bfloat16)


def attend_pallas(query_rows, key_blocks, entries, global_block, gain_query, gain_key, gain_out):
    meta = jnp.concatenate([entries.astype(jnp.int32), jnp.reshape(global_block, (1,)).astype(jnp.int32)])
    lanes = GROUP * HD

    def row_spec(block, rows=BLOCK):
        return pl.BlockSpec((rows, lanes), lambda g, meta: (block, g))

    gain_spec = pl.BlockSpec((1, lanes), lambda g, meta: (0, g))
    grid_spec = pltpu.PrefetchScalarGridSpec(
        num_scalar_prefetch=1,
        grid=(HEADS // GROUP,),
        in_specs=[row_spec(0)] + [row_spec(block, rows) for _, block, rows in key_blocks] + [gain_spec] * 3,
        out_specs=row_spec(0),
    )
    return pl.pallas_call(
        attend_kernel,
        grid_spec=grid_spec,
        out_shape=jax.ShapeDtypeStruct((BLOCK, WIDTH), jnp.bfloat16),
    )(
        meta,
        query_rows,
        *[array for array, _, _ in key_blocks],
        gain_query.reshape(1, WIDTH),
        gain_key.reshape(1, WIDTH),
        gain_out.reshape(1, WIDTH),
    )


def local(earlier_span, span_inputs, next_inputs, block_list, q_gain, k_gain, out_gain):
    group_size = lax.axis_size("ctx")
    sections = lax.axis_size("section")
    position = lax.axis_index("ctx")
    section_pos = lax.axis_index("section")
    query_entries = lax.dynamic_index_in_dim(block_list, position, 0, keepdims=False)
    full_entries = block_list[group_size - 1]
    global_block = group_size + position
    gain_query = q_gain[0]
    gain_key = k_gain[0]
    gain_out = out_gain[0]
    last = position == group_size - 1

    first_earlier = earlier_span[0]
    first_current = span_inputs[0]
    root = full_entries[LOCAL] % group_size
    piece_one = scatter_piece(jnp.concatenate([first_earlier, first_current]), "ctx", root)
    behind = jnp.where(last, first_earlier, first_current)
    front = shifted(behind[: BLOCK // 2], "ctx", 1)
    piece_one, front = lax.optimization_barrier((piece_one, front))
    back = shifted(behind[BLOCK // 2 :], "ctx", 1)
    both = gather_pieces(piece_one, "ctx")
    both, back = lax.optimization_barrier((both, back))
    held, both = lax.optimization_barrier((jnp.where(last, first_current, next_inputs), both))
    previous_early = shifted(held, "ctx", 1)

    half = BLOCK // 2
    key_one = (
        (first_current, 0, BLOCK),
        (front, 0, half),
        (back, 0, half),
        (both, 0, BLOCK),
        (both, 1, BLOCK),
    )
    first_result = attend_pallas(
        first_current, key_one, query_entries, global_block, gain_query, gain_key, gain_out
    )

    later_root = full_entries[LOCAL + NR] % group_size
    source = jnp.where(section_pos == sections - 1, next_inputs, first_result)
    source, previous_early = lax.optimization_barrier((source, previous_early))
    piece = shifted(scatter_piece(source, "ctx", later_root), "section", 1)
    outgoing, piece = lax.optimization_barrier((first_result, piece))
    straight = [(s, s + 1) for s in range(sections - 1)]
    received = lax.ppermute(outgoing, "section", straight)
    diagonal = [
        (s * group_size + i, (s + 1) * group_size + i + 1)
        for s in range(sections - 1)
        for i in range(group_size - 1)
    ]
    received_previous = lax.ppermute(outgoing, ("section", "ctx"), diagonal)
    strided_later = gather_pieces(piece, "ctx")
    second_current = jnp.where(section_pos == 0, next_inputs, received)
    previous_two = jnp.where(
        (position == 0) | (section_pos == 0), previous_early, received_previous
    )
    key_two = (
        (second_current, 0, BLOCK),
        (previous_two, 0, half),
        (previous_two, 1, half),
        (both, 1, BLOCK),
        (strided_later, 0, BLOCK),
    )
    second_result = attend_pallas(
        second_current, key_two, query_entries, global_block, gain_query, gain_key, gain_out
    )
    return second_result[None]


def solution(mesh):
    in_specs = (
        P("section", "ctx", None),
        P("section", "ctx", None),
        P("ctx", None),
        P(),
        P("section", None),
        P("section", None),
        P("section", None),
    )
    out_specs = P("section", "ctx", None)
    return jax.shard_map(local, mesh=mesh, in_specs=in_specs, out_specs=out_specs, check_vma=False)
```

```python
import jax
import jax.numpy as jnp
from jax import lax
from jax.sharding import PartitionSpec as P
from jax.experimental import pallas as pl
from jax.experimental.pallas import tpu as pltpu
import functools

HEADS = 32
HD = 128
BLOCK = 128
LOCAL = 2
NR = 1
WIDTH = 4096
NSEL = 4
GROUP = 8


def shifted(value, axis, steps):
    count = lax.axis_size(axis)
    pairs = [(source, (source + steps) % count) for source in range(count)]
    return lax.ppermute(value, axis, pairs)


def scatter_piece(payload, axis, root):
    count = lax.axis_size(axis)
    rows = payload.shape[0]
    pieces = payload.reshape(count, rows // count, payload.shape[1])
    received = lax.all_to_all(pieces, axis, 0, 0, tiled=True)
    return lax.dynamic_index_in_dim(received, root, 0, keepdims=True)


def gather_pieces(piece, axis):
    count = lax.axis_size(axis)
    shape = (count,) + piece.shape[1:]
    gathered = lax.all_to_all(jnp.broadcast_to(piece, shape), axis, 0, 0, tiled=True)
    return gathered.reshape(count * piece.shape[1], piece.shape[2])


def attend_kernel(meta_ref, q_ref, k0_ref, k1a_ref, k1b_ref, k2_ref, k3_ref, gq_ref, gk_ref, go_ref, out_ref):
    key_refs = (k0_ref, (k1a_ref, k1b_ref), k2_ref, k3_ref)

    def key_rows(b, lanes):
        ref = key_refs[b]
        if isinstance(ref, tuple):
            return jnp.concatenate([part[:, lanes] for part in ref], axis=0)
        return ref[:, lanes]

    global_block = meta_ref[NSEL]
    query_pos = lax.broadcasted_iota(jnp.int32, (BLOCK, BLOCK), 0)
    key_pos = lax.broadcasted_iota(jnp.int32, (BLOCK, BLOCK), 1)
    allowed = []
    for b in range(NSEL):
        entry = meta_ref[b]
        allowed.append((entry >= 0) & ((entry != global_block) | (key_pos <= query_pos)))
    for h in range(GROUP):
        lanes = slice(h * HD, (h + 1) * HD)
        rows = q_ref[:, lanes].astype(jnp.float32)
        normed = rows * lax.rsqrt(jnp.mean(rows * rows, axis=-1, keepdims=True) + 1e-06)
        queries = (normed * gq_ref[:, lanes] * HD ** (-0.5)).astype(jnp.bfloat16)
        scores = []
        values = [key_rows(b, lanes) for b in range(NSEL)]
        for b in range(NSEL):
            raw_keys = values[b]
            wide = raw_keys.astype(jnp.float32)
            keys = (wide * lax.rsqrt(jnp.mean(wide * wide, axis=-1, keepdims=True) + 1e-06) * gk_ref[:, lanes]).astype(jnp.bfloat16)
            s = lax.dot_general(queries, keys, (((1,), (1,)), ((), ())), preferred_element_type=jnp.float32)
            scores.append(jnp.where(allowed[b], s, -jnp.inf))
        maxima = functools.reduce(jnp.maximum, [jnp.max(s, axis=-1, keepdims=True) for s in scores])
        raws = [jnp.exp(s - maxima) for s in scores]
        totals = functools.reduce(jnp.add, [jnp.sum(r, axis=-1, keepdims=True) for r in raws])
        context = None
        for b in range(NSEL):
            part = jnp.dot(raws[b].astype(jnp.bfloat16), values[b], preferred_element_type=jnp.float32)
            context = part if context is None else context + part
        out_ref[:, lanes] = (rows + go_ref[:, lanes] * (context / totals)).astype(jnp.bfloat16)


def attend_pallas(query_rows, key_blocks, entries, global_block, gain_query, gain_key, gain_out):
    meta = jnp.concatenate([entries.astype(jnp.int32), jnp.reshape(global_block, (1,)).astype(jnp.int32)])
    lanes = GROUP * HD

    def row_spec(block, rows=BLOCK):
        return pl.BlockSpec((rows, lanes), lambda g, meta: (block, g))

    gain_spec = pl.BlockSpec((1, lanes), lambda g, meta: (0, g))
    grid_spec = pltpu.PrefetchScalarGridSpec(
        num_scalar_prefetch=1,
        grid=(HEADS // GROUP,),
        in_specs=[row_spec(0)] + [row_spec(block, rows) for _, block, rows in key_blocks] + [gain_spec] * 3,
        out_specs=row_spec(0),
    )
    return pl.pallas_call(
        attend_kernel,
        grid_spec=grid_spec,
        out_shape=jax.ShapeDtypeStruct((BLOCK, WIDTH), jnp.bfloat16),
    )(
        meta,
        query_rows,
        *[array for array, _, _ in key_blocks],
        gain_query.reshape(1, WIDTH),
        gain_key.reshape(1, WIDTH),
        gain_out.reshape(1, WIDTH),
    )


def local(earlier_span, span_inputs, next_inputs, block_list, q_gain, k_gain, out_gain):
    group_size = lax.axis_size("ctx")
    sections = lax.axis_size("section")
    position = lax.axis_index("ctx")
    section_pos = lax.axis_index("section")
    query_entries = lax.dynamic_index_in_dim(block_list, position, 0, keepdims=False)
    full_entries = block_list[group_size - 1]
    global_block = group_size + position
    gain_query = q_gain[0]
    gain_key = k_gain[0]
    gain_out = out_gain[0]
    last = position == group_size - 1

    first_earlier = earlier_span[0]
    first_current = span_inputs[0]
    root = full_entries[LOCAL] % group_size
    piece_one = scatter_piece(jnp.concatenate([first_earlier, first_current]), "ctx", root)
    previous_one = shifted(jnp.where(last, first_earlier, first_current), "ctx", 1)
    piece_one, previous_one = lax.optimization_barrier((piece_one, previous_one))
    both = gather_pieces(piece_one, "ctx")
    half = BLOCK // 2

    own_keys = (
        (first_current, 0, BLOCK),
        (previous_one, 0, half),
        (previous_one, 1, half),
        (first_earlier, 0, BLOCK),
        (first_earlier, 0, BLOCK),
    )
    own_result = attend_pallas(
        first_current, own_keys, query_entries, global_block, gain_query, gain_key, gain_out
    )
    later_root = full_entries[LOCAL + NR] % group_size
    source = jnp.where(section_pos == sections - 1, next_inputs, own_result)
    piece = shifted(scatter_piece(source, "ctx", later_root), "section", 1)
    strided_later = gather_pieces(piece, "ctx")

    held, both = lax.optimization_barrier((jnp.where(last, first_current, next_inputs), both))
    previous_early = shifted(held, "ctx", 1)

    key_one = (
        (first_current, 0, BLOCK),
        (previous_one, 0, half),
        (previous_one, 1, half),
        (both, 0, BLOCK),
        (both, 1, BLOCK),
    )
    first_result = attend_pallas(
        first_current, key_one, query_entries, global_block, gain_query, gain_key, gain_out
    )

    straight = [(s, s + 1) for s in range(sections - 1)]
    received = lax.ppermute(first_result, "section", straight)
    diagonal = [
        (s * group_size + i, (s + 1) * group_size + i + 1)
        for s in range(sections - 1)
        for i in range(group_size - 1)
    ]
    received_previous = lax.ppermute(first_result, ("section", "ctx"), diagonal)
    second_current = jnp.where(section_pos == 0, next_inputs, received)
    previous_two = jnp.where(
        (position == 0) | (section_pos == 0), previous_early, received_previous
    )
    key_two = (
        (second_current, 0, BLOCK),
        (previous_two, 0, half),
        (previous_two, 1, half),
        (both, 1, BLOCK),
        (strided_later, 0, BLOCK),
    )
    second_result = attend_pallas(
        second_current, key_two, query_entries, global_block, gain_query, gain_key, gain_out
    )
    return second_result[None]


def solution(mesh):
    in_specs = (
        P("section", "ctx", None),
        P("section", "ctx", None),
        P("ctx", None),
        P(),
        P("section", None),
        P("section", None),
        P("section", None),
    )
    out_specs = P("section", "ctx", None)
    return jax.shard_map(local, mesh=mesh, in_specs=in_specs, out_specs=out_specs, check_vma=False)
```

```python
import jax
import jax.numpy as jnp
from jax import lax
from jax.sharding import PartitionSpec as P
from jax.experimental import pallas as pl
from jax.experimental.pallas import tpu as pltpu
import functools

HEADS = 32
HD = 128
BLOCK = 128
LOCAL = 2
NR = 1
WIDTH = 4096
NSEL = 4
GROUP = 16


def shifted(value, axis, steps):
    count = lax.axis_size(axis)
    pairs = [(source, (source + steps) % count) for source in range(count)]
    return lax.ppermute(value, axis, pairs)


def scatter_piece(payload, axis, root):
    count = lax.axis_size(axis)
    rows = payload.shape[0]
    pieces = payload.reshape(count, rows // count, payload.shape[1])
    received = lax.all_to_all(pieces, axis, 0, 0, tiled=True)
    return lax.dynamic_index_in_dim(received, root, 0, keepdims=True)


def gather_pieces(piece, axis):
    count = lax.axis_size(axis)
    shape = (count,) + piece.shape[1:]
    gathered = lax.all_to_all(jnp.broadcast_to(piece, shape), axis, 0, 0, tiled=True)
    return gathered.reshape(count * piece.shape[1], piece.shape[2])


def attend_kernel(meta_ref, q_ref, k0_ref, k1a_ref, k1b_ref, k2_ref, k3_ref, gq_ref, gk_ref, go_ref, out_ref):
    key_refs = (k0_ref, (k1a_ref, k1b_ref), k2_ref, k3_ref)

    def key_rows(b, lanes):
        ref = key_refs[b]
        if isinstance(ref, tuple):
            return jnp.concatenate([part[:, lanes] for part in ref], axis=0)
        return ref[:, lanes]

    global_block = meta_ref[NSEL]
    query_pos = lax.broadcasted_iota(jnp.int32, (BLOCK, BLOCK), 0)
    key_pos = lax.broadcasted_iota(jnp.int32, (BLOCK, BLOCK), 1)
    entry = meta_ref[0]
    allowed = (entry >= 0) & ((entry != global_block) | (key_pos <= query_pos))
    biases = [None] + [
        jnp.where((meta_ref[b] >= 0) & (meta_ref[b] != global_block), 0.0, -jnp.inf).astype(jnp.float32)
        for b in range(1, NSEL)
    ]
    for h in range(GROUP):
        lanes = slice(h * HD, (h + 1) * HD)
        rows = q_ref[:, lanes].astype(jnp.float32)
        normed = rows * lax.rsqrt(jnp.mean(rows * rows, axis=-1, keepdims=True) + 1e-06)
        queries = (normed * gq_ref[:, lanes] * HD ** (-0.5)).astype(jnp.bfloat16)
        scores = []
        values = [key_rows(b, lanes) for b in range(NSEL)]
        for b in range(NSEL):
            raw_keys = values[b]
            wide = raw_keys.astype(jnp.float32)
            keys = (wide * lax.rsqrt(jnp.mean(wide * wide, axis=-1, keepdims=True) + 1e-06) * gk_ref[:, lanes]).astype(jnp.bfloat16)
            s = lax.dot_general(queries, keys, (((1,), (1,)), ((), ())), preferred_element_type=jnp.float32)
            scores.append(jnp.where(allowed, s, -jnp.inf) if b == 0 else s)
        peaks = [jnp.max(s, axis=-1, keepdims=True) for s in scores]
        maxima = functools.reduce(
            jnp.maximum, [peaks[0]] + [peaks[b] + biases[b] for b in range(1, NSEL)]
        )
        raws = [jnp.exp(scores[0] - maxima)] + [
            jnp.exp(scores[b] - (maxima - biases[b])) for b in range(1, NSEL)
        ]
        totals = functools.reduce(jnp.add, [jnp.sum(r, axis=-1, keepdims=True) for r in raws])
        context = None
        for b in range(NSEL):
            part = jnp.dot(raws[b].astype(jnp.bfloat16), values[b], preferred_element_type=jnp.float32)
            context = part if context is None else context + part
        out_ref[:, lanes] = (rows + go_ref[:, lanes] * (context / totals)).astype(jnp.bfloat16)


def attend_pallas(query_rows, key_blocks, entries, global_block, gain_query, gain_key, gain_out):
    meta = jnp.concatenate([entries.astype(jnp.int32), jnp.reshape(global_block, (1,)).astype(jnp.int32)])
    lanes = GROUP * HD

    def row_spec(block, rows=BLOCK):
        return pl.BlockSpec((rows, lanes), lambda g, meta: (block, g))

    gain_spec = pl.BlockSpec((1, lanes), lambda g, meta: (0, g))
    grid_spec = pltpu.PrefetchScalarGridSpec(
        num_scalar_prefetch=1,
        grid=(HEADS // GROUP,),
        in_specs=[row_spec(0)] + [row_spec(block, rows) for _, block, rows in key_blocks] + [gain_spec] * 3,
        out_specs=row_spec(0),
    )
    return pl.pallas_call(
        attend_kernel,
        grid_spec=grid_spec,
        out_shape=jax.ShapeDtypeStruct((BLOCK, WIDTH), jnp.bfloat16),
    )(
        meta,
        query_rows,
        *[array for array, _, _ in key_blocks],
        gain_query.reshape(1, WIDTH),
        gain_key.reshape(1, WIDTH),
        gain_out.reshape(1, WIDTH),
    )


def local(earlier_span, span_inputs, next_inputs, block_list, q_gain, k_gain, out_gain):
    group_size = lax.axis_size("ctx")
    sections = lax.axis_size("section")
    position = lax.axis_index("ctx")
    section_pos = lax.axis_index("section")
    query_entries = lax.dynamic_index_in_dim(block_list, position, 0, keepdims=False)
    full_entries = block_list[group_size - 1]
    global_block = group_size + position
    gain_query = q_gain[0]
    gain_key = k_gain[0]
    gain_out = out_gain[0]
    last = position == group_size - 1

    first_earlier = earlier_span[0]
    first_current = span_inputs[0]
    root = full_entries[LOCAL] % group_size
    piece_one = scatter_piece(jnp.concatenate([first_earlier, first_current]), "ctx", root)
    behind = jnp.where(last, first_earlier, first_current)
    front = shifted(behind[: BLOCK // 2], "ctx", 1)
    piece_one, front = lax.optimization_barrier((piece_one, front))
    back = shifted(behind[BLOCK // 2 :], "ctx", 1)
    both = gather_pieces(piece_one, "ctx")
    both, back = lax.optimization_barrier((both, back))
    held, both = lax.optimization_barrier((jnp.where(last, first_current, next_inputs), both))
    previous_early = shifted(held, "ctx", 1)

    half = BLOCK // 2
    key_one = (
        (first_current, 0, BLOCK),
        (front, 0, half),
        (back, 0, half),
        (both, 0, BLOCK),
        (both, 1, BLOCK),
    )
    first_result = attend_pallas(
        first_current, key_one, query_entries, global_block, gain_query, gain_key, gain_out
    )

    later_root = full_entries[LOCAL + NR] % group_size
    source = jnp.where(section_pos == sections - 1, next_inputs, first_result)
    source, previous_early = lax.optimization_barrier((source, previous_early))
    piece = shifted(scatter_piece(source, "ctx", later_root), "section", 1)
    outgoing, piece = lax.optimization_barrier((first_result, piece))
    straight = [(s, s + 1) for s in range(sections - 1)]
    received = lax.ppermute(outgoing, "section", straight)
    diagonal = [
        (s * group_size + i, (s + 1) * group_size + i + 1)
        for s in range(sections - 1)
        for i in range(group_size - 1)
    ]
    received_previous = lax.ppermute(outgoing, ("section", "ctx"), diagonal)
    strided_later = gather_pieces(piece, "ctx")
    second_current = jnp.where(section_pos == 0, next_inputs, received)
    previous_two = jnp.where(
        (position == 0) | (section_pos == 0), previous_early, received_previous
    )
    key_two = (
        (second_current, 0, BLOCK),
        (previous_two, 0, half),
        (previous_two, 1, half),
        (both, 1, BLOCK),
        (strided_later, 0, BLOCK),
    )
    second_result = attend_pallas(
        second_current, key_two, query_entries, global_block, gain_query, gain_key, gain_out
    )
    return second_result[None]


def solution(mesh):
    in_specs = (
        P("section", "ctx", None),
        P("section", "ctx", None),
        P("ctx", None),
        P(),
        P("section", None),
        P("section", None),
        P("section", None),
    )
    out_specs = P("section", "ctx", None)
    return jax.shard_map(local, mesh=mesh, in_specs=in_specs, out_specs=out_specs, check_vma=False)
```

```python
import jax
import jax.numpy as jnp
from jax import lax
from jax.sharding import PartitionSpec as P
from jax.experimental import pallas as pl
from jax.experimental.pallas import tpu as pltpu
import functools

HEADS = 32
HD = 128
BLOCK = 128
LOCAL = 2
NR = 1
WIDTH = 4096
NSEL = 4
GROUP = 8


def shifted(value, axis, steps):
    count = lax.axis_size(axis)
    pairs = [(source, (source + steps) % count) for source in range(count)]
    return lax.ppermute(value, axis, pairs)


def scatter_piece(payloads, axis, root):
    count = lax.axis_size(axis)
    rows = sum(payload.shape[0] for payload in payloads) // count
    pieces = jnp.concatenate([payload.reshape(-1, rows, payload.shape[1]) for payload in payloads])
    received = lax.all_to_all(pieces, axis, 0, 0, tiled=True)
    return lax.dynamic_index_in_dim(received, root, 0, keepdims=True)


def gather_pieces(piece, axis):
    count = lax.axis_size(axis)
    shape = (count,) + piece.shape[1:]
    gathered = lax.all_to_all(jnp.broadcast_to(piece, shape), axis, 0, 0, tiled=True)
    return gathered.reshape(count * piece.shape[1], piece.shape[2])


def attend_kernel(meta_ref, q_ref, k0_ref, k1a_ref, k1b_ref, k2_ref, k3_ref, gq_ref, gk_ref, go_ref, out_ref):
    key_refs = (k0_ref, (k1a_ref, k1b_ref), k2_ref, k3_ref)

    def key_rows(b, lanes):
        ref = key_refs[b]
        if isinstance(ref, tuple):
            return jnp.concatenate([part[:, lanes] for part in ref], axis=0)
        return ref[:, lanes]

    global_block = meta_ref[NSEL]
    query_pos = lax.broadcasted_iota(jnp.int32, (BLOCK, BLOCK), 0)
    key_pos = lax.broadcasted_iota(jnp.int32, (BLOCK, BLOCK), 1)
    allowed = []
    for b in range(NSEL):
        entry = meta_ref[b]
        allowed.append((entry >= 0) & ((entry != global_block) | (key_pos <= query_pos)))
    for h in range(GROUP):
        lanes = slice(h * HD, (h + 1) * HD)
        rows = q_ref[:, lanes].astype(jnp.float32)
        normed = rows * lax.rsqrt(jnp.mean(rows * rows, axis=-1, keepdims=True) + 1e-06)
        queries = (normed * gq_ref[:, lanes] * HD ** (-0.5)).astype(jnp.bfloat16)
        scores = []
        values = [key_rows(b, lanes) for b in range(NSEL)]
        for b in range(NSEL):
            raw_keys = values[b]
            wide = raw_keys.astype(jnp.float32)
            keys = (wide * lax.rsqrt(jnp.mean(wide * wide, axis=-1, keepdims=True) + 1e-06) * gk_ref[:, lanes]).astype(jnp.bfloat16)
            s = lax.dot_general(queries, keys, (((1,), (1,)), ((), ())), preferred_element_type=jnp.float32)
            scores.append(jnp.where(allowed[b], s, -jnp.inf))
        maxima = functools.reduce(jnp.maximum, [jnp.max(s, axis=-1, keepdims=True) for s in scores])
        raws = [jnp.exp(s - maxima) for s in scores]
        totals = functools.reduce(jnp.add, [jnp.sum(r, axis=-1, keepdims=True) for r in raws])
        context = None
        for b in range(NSEL):
            part = jnp.dot(raws[b].astype(jnp.bfloat16), values[b], preferred_element_type=jnp.float32)
            context = part if context is None else context + part
        out_ref[:, lanes] = (rows + go_ref[:, lanes] * (context / totals)).astype(jnp.bfloat16)


def attend_pallas(query_rows, key_blocks, entries, global_block, gain_query, gain_key, gain_out):
    meta = jnp.concatenate([entries.astype(jnp.int32), jnp.reshape(global_block, (1,)).astype(jnp.int32)])
    lanes = GROUP * HD

    def row_spec(block, rows=BLOCK):
        return pl.BlockSpec((rows, lanes), lambda g, meta: (block, g))

    gain_spec = pl.BlockSpec((1, lanes), lambda g, meta: (0, g))
    grid_spec = pltpu.PrefetchScalarGridSpec(
        num_scalar_prefetch=1,
        grid=(HEADS // GROUP,),
        in_specs=[row_spec(0)] + [row_spec(block, rows) for _, block, rows in key_blocks] + [gain_spec] * 3,
        out_specs=row_spec(0),
    )
    return pl.pallas_call(
        attend_kernel,
        grid_spec=grid_spec,
        out_shape=jax.ShapeDtypeStruct((BLOCK, WIDTH), jnp.bfloat16),
    )(
        meta,
        query_rows,
        *[array for array, _, _ in key_blocks],
        gain_query.reshape(1, WIDTH),
        gain_key.reshape(1, WIDTH),
        gain_out.reshape(1, WIDTH),
    )


def local(earlier_span, span_inputs, next_inputs, block_list, q_gain, k_gain, out_gain):
    group_size = lax.axis_size("ctx")
    sections = lax.axis_size("section")
    position = lax.axis_index("ctx")
    section_pos = lax.axis_index("section")
    query_entries = lax.dynamic_index_in_dim(block_list, position, 0, keepdims=False)
    full_entries = block_list[group_size - 1]
    global_block = group_size + position
    gain_query = q_gain[0]
    gain_key = k_gain[0]
    gain_out = out_gain[0]
    last = position == group_size - 1

    first_earlier = earlier_span[0]
    first_current = span_inputs[0]
    root = full_entries[LOCAL] % group_size
    piece_one = scatter_piece([first_earlier, first_current], "ctx", root)
    behind = jnp.where(last, first_earlier, first_current)
    front = shifted(behind[: BLOCK // 2], "ctx", 1)
    piece_one, front = lax.optimization_barrier((piece_one, front))
    back = shifted(behind[BLOCK // 2 :], "ctx", 1)
    both = gather_pieces(piece_one, "ctx")
    both, back = lax.optimization_barrier((both, back))
    held, both = lax.optimization_barrier((jnp.where(last, first_current, next_inputs), both))
    previous_early = shifted(held, "ctx", 1)

    half = BLOCK // 2
    key_one = (
        (first_current, 0, BLOCK),
        (front, 0, half),
        (back, 0, half),
        (both, 0, BLOCK),
        (both, 1, BLOCK),
    )
    first_result = attend_pallas(
        first_current, key_one, query_entries, global_block, gain_query, gain_key, gain_out
    )

    later_root = full_entries[LOCAL + NR] % group_size
    source = jnp.where(section_pos == sections - 1, next_inputs, first_result)
    source, previous_early = lax.optimization_barrier((source, previous_early))
    piece = shifted(scatter_piece([source], "ctx", later_root), "section", 1)
    outgoing, piece = lax.optimization_barrier((first_result, piece))
    straight = [(s, s + 1) for s in range(sections - 1)]
    received = lax.ppermute(outgoing, "section", straight)
    diagonal = [
        (s * group_size + i, (s + 1) * group_size + i + 1)
        for s in range(sections - 1)
        for i in range(group_size - 1)
    ]
    received_previous = lax.ppermute(outgoing, ("section", "ctx"), diagonal)
    strided_later = gather_pieces(piece, "ctx")
    second_current = jnp.where(section_pos == 0, next_inputs, received)
    previous_two = jnp.where(
        (position == 0) | (section_pos == 0), previous_early, received_previous
    )
    key_two = (
        (second_current, 0, BLOCK),
        (previous_two, 0, half),
        (previous_two, 1, half),
        (both, 1, BLOCK),
        (strided_later, 0, BLOCK),
    )
    second_result = attend_pallas(
        second_current, key_two, query_entries, global_block, gain_query, gain_key, gain_out
    )
    return second_result[None]


def solution(mesh):
    in_specs = (
        P("section", "ctx", None),
        P("section", "ctx", None),
        P("ctx", None),
        P(),
        P("section", None),
        P("section", None),
        P("section", None),
    )
    out_specs = P("section", "ctx", None)
    return jax.shard_map(local, mesh=mesh, in_specs=in_specs, out_specs=out_specs, check_vma=False)
```

```python
import jax
import jax.numpy as jnp
from jax import lax
from jax.sharding import PartitionSpec as P
from jax.experimental import pallas as pl
from jax.experimental.pallas import tpu as pltpu
import functools

HEADS = 32
HD = 128
BLOCK = 128
LOCAL = 2
NR = 1
WIDTH = 4096
NSEL = 4
GROUP = 8


def shifted(value, axis, steps):
    count = lax.axis_size(axis)
    pairs = [(source, (source + steps) % count) for source in range(count)]
    return lax.ppermute(value, axis, pairs)


def scatter_piece(payload, axis, root):
    count = lax.axis_size(axis)
    rows = payload.shape[0]
    pieces = payload.reshape(count, rows // count, payload.shape[1])
    received = lax.all_to_all(pieces, axis, 0, 0, tiled=True)
    return lax.dynamic_index_in_dim(received, root, 0, keepdims=True)


def gather_pieces(piece, axis):
    count = lax.axis_size(axis)
    shape = (count,) + piece.shape[1:]
    gathered = lax.all_to_all(jnp.broadcast_to(piece, shape), axis, 0, 0, tiled=True)
    return gathered.reshape(count * piece.shape[1], piece.shape[2])


def attend_kernel(meta_ref, q_ref, k0_ref, k1a_ref, k1b_ref, k2_ref, k3_ref, gq_ref, gk_ref, go_ref, out_ref):
    key_refs = (k0_ref, (k1a_ref, k1b_ref), k2_ref, k3_ref)

    def key_rows(b, lanes):
        ref = key_refs[b]
        if isinstance(ref, tuple):
            return jnp.concatenate([part[:, lanes] for part in ref], axis=0)
        return ref[:, lanes]

    global_block = meta_ref[NSEL]
    query_pos = lax.broadcasted_iota(jnp.int32, (BLOCK, BLOCK), 0)
    key_pos = lax.broadcasted_iota(jnp.int32, (BLOCK, BLOCK), 1)
    entry = meta_ref[0]
    allowed = (entry >= 0) & ((entry != global_block) | (key_pos <= query_pos))
    biases = [None] + [
        jnp.where((meta_ref[b] >= 0) & (meta_ref[b] != global_block), 0.0, -jnp.inf).astype(jnp.float32)
        for b in range(1, NSEL)
    ]
    for h in range(GROUP):
        lanes = slice(h * HD, (h + 1) * HD)
        rows = q_ref[:, lanes].astype(jnp.float32)
        normed = rows * lax.rsqrt(jnp.mean(rows * rows, axis=-1, keepdims=True) + 1e-06)
        queries = (normed * gq_ref[:, lanes] * HD ** (-0.5)).astype(jnp.bfloat16)
        scores = []
        values = [key_rows(b, lanes) for b in range(NSEL)]
        for b in range(NSEL):
            raw_keys = values[b]
            wide = raw_keys.astype(jnp.float32)
            keys = (wide * lax.rsqrt(jnp.mean(wide * wide, axis=-1, keepdims=True) + 1e-06) * gk_ref[:, lanes]).astype(jnp.bfloat16)
            s = lax.dot_general(queries, keys, (((1,), (1,)), ((), ())), preferred_element_type=jnp.float32)
            scores.append(jnp.where(allowed, s, -jnp.inf) if b == 0 else s)
        peaks = [jnp.max(s, axis=-1, keepdims=True) for s in scores]
        maxima = functools.reduce(
            jnp.maximum, [peaks[0]] + [peaks[b] + biases[b] for b in range(1, NSEL)]
        )
        raws = [jnp.exp(scores[0] - maxima)] + [
            jnp.exp(scores[b] - (maxima - biases[b])) for b in range(1, NSEL)
        ]
        totals = functools.reduce(jnp.add, [jnp.sum(r, axis=-1, keepdims=True) for r in raws])
        context = None
        for b in range(NSEL):
            part = jnp.dot(raws[b].astype(jnp.bfloat16), values[b], preferred_element_type=jnp.float32)
            context = part if context is None else context + part
        out_ref[:, lanes] = (rows + go_ref[:, lanes] * (context / totals)).astype(jnp.bfloat16)


def attend_pallas(query_rows, key_blocks, entries, global_block, gain_query, gain_key, gain_out):
    meta = jnp.concatenate([entries.astype(jnp.int32), jnp.reshape(global_block, (1,)).astype(jnp.int32)])
    lanes = GROUP * HD

    def row_spec(block, rows=BLOCK):
        return pl.BlockSpec((rows, lanes), lambda g, meta: (block, g))

    gain_spec = pl.BlockSpec((1, lanes), lambda g, meta: (0, g))
    grid_spec = pltpu.PrefetchScalarGridSpec(
        num_scalar_prefetch=1,
        grid=(HEADS // GROUP,),
        in_specs=[row_spec(0)] + [row_spec(block, rows) for _, block, rows in key_blocks] + [gain_spec] * 3,
        out_specs=row_spec(0),
    )
    return pl.pallas_call(
        attend_kernel,
        grid_spec=grid_spec,
        out_shape=jax.ShapeDtypeStruct((BLOCK, WIDTH), jnp.bfloat16),
    )(
        meta,
        query_rows,
        *[array for array, _, _ in key_blocks],
        gain_query.reshape(1, WIDTH),
        gain_key.reshape(1, WIDTH),
        gain_out.reshape(1, WIDTH),
    )


def local(earlier_span, span_inputs, next_inputs, block_list, q_gain, k_gain, out_gain):
    group_size = lax.axis_size("ctx")
    sections = lax.axis_size("section")
    position = lax.axis_index("ctx")
    section_pos = lax.axis_index("section")
    query_entries = lax.dynamic_index_in_dim(block_list, position, 0, keepdims=False)
    full_entries = block_list[group_size - 1]
    global_block = group_size + position
    gain_query = q_gain[0]
    gain_key = k_gain[0]
    gain_out = out_gain[0]
    last = position == group_size - 1

    first_earlier = earlier_span[0]
    first_current = span_inputs[0]
    root = full_entries[LOCAL] % group_size
    piece_one = scatter_piece(jnp.concatenate([first_earlier, first_current]), "ctx", root)
    behind = jnp.where(last, first_earlier, first_current)
    front = shifted(behind[: BLOCK // 2], "ctx", 1)
    piece_one, front = lax.optimization_barrier((piece_one, front))
    back = shifted(behind[BLOCK // 2 :], "ctx", 1)
    both = gather_pieces(piece_one, "ctx")
    both, back = lax.optimization_barrier((both, back))
    held, both = lax.optimization_barrier((jnp.where(last, first_current, next_inputs), both))
    previous_early = shifted(held, "ctx", 1)

    half = BLOCK // 2
    key_one = (
        (first_current, 0, BLOCK),
        (front, 0, half),
        (back, 0, half),
        (both, 0, BLOCK),
        (both, 1, BLOCK),
    )
    first_result = attend_pallas(
        first_current, key_one, query_entries, global_block, gain_query, gain_key, gain_out
    )

    later_root = full_entries[LOCAL + NR] % group_size
    source = jnp.where(section_pos == sections - 1, next_inputs, first_result)
    source, previous_early = lax.optimization_barrier((source, previous_early))
    piece = shifted(scatter_piece(source, "ctx", later_root), "section", 1)
    outgoing, piece = lax.optimization_barrier((first_result, piece))
    straight = [(s, s + 1) for s in range(sections - 1)]
    received = lax.ppermute(outgoing, "section", straight)
    diagonal = [
        (s * group_size + i, (s + 1) * group_size + i + 1)
        for s in range(sections - 1)
        for i in range(group_size - 1)
    ]
    received_previous = lax.ppermute(outgoing, ("section", "ctx"), diagonal)
    strided_later = gather_pieces(piece, "ctx")
    second_current = jnp.where(section_pos == 0, next_inputs, received)
    previous_two = jnp.where(
        (position == 0) | (section_pos == 0), previous_early, received_previous
    )
    key_two = (
        (second_current, 0, BLOCK),
        (previous_two, 0, half),
        (previous_two, 1, half),
        (both, 1, BLOCK),
        (strided_later, 0, BLOCK),
    )
    second_result = attend_pallas(
        second_current, key_two, query_entries, global_block, gain_query, gain_key, gain_out
    )
    return second_result[None]


def solution(mesh):
    in_specs = (
        P("section", "ctx", None),
        P("section", "ctx", None),
        P("ctx", None),
        P(),
        P("section", None),
        P("section", None),
        P("section", None),
    )
    out_specs = P("section", "ctx", None)
    return jax.shard_map(local, mesh=mesh, in_specs=in_specs, out_specs=out_specs, check_vma=False)
```
